512 devices in a mesh: dp: 16 (over z), row: 4 (over y), col: 8 (over x, core).
Axes of the slice: x: 4, y: 4, z: 16, core: 2. Of those that a mesh axis runs over, the one named last changes fastest.
Arguments:
- layer_input: bfloat16 [3072, 4096], P(('dp', 'col'), 'row'), may hold values from -6 to 6
- hidden_grad: bfloat16 [3072, 14336], P(('dp', 'row'), 'col'), may hold values from -6 to 6
- gate_slots: bfloat16 [4, 8, 48, 128, 128], P('row', 'col', 'dp'), may hold values from -0.125 to 0.125
- up_slots: bfloat16 [4, 8, 48, 128, 128], P('row', 'col', 'dp'), may hold values from -0.125 to 0.125
- block_mask: int32 [32, 112], replicated, may hold values from 0 to 1, as said below
Outputs:
- input_grad: bfloat16 [3072, 4096], P(('dp', 'col'), 'row')
- gate_slot_grad: float32 [4, 8, 48, 128, 128], P('row', 'col', 'dp')
- up_slot_grad: float32 [4, 8, 48, 128, 128], P('row', 'col', 'dp')
The draws below stay inside these ranges and needn't reach their ends.
Inputs may be any that keep to these rules, and one draw needn't show every extreme that they name: `block_mask`: every tile of 8 x 14 blocks keeps between 24 and 48 blocks; some tile keeps exactly 48, which tile depends on the draw.
All inputs are finite; a program needn't handle non-finite values.
Results may differ from the reference program's by a relative error of at most 0.022.
Values may be sent and summed in bfloat16 or wider, within the bound.
No kernel may reach another device: no remote copies, remote signals or barrier semaphores. Data moves between devices by JAX's collectives and lax.ppermute only.
A program may use at most 64 MiB of HBM per device.

```python
import jax
import jax.numpy as jnp
from jax import lax

D = 4096
FF = 14336
BS = 128
TOK = 192
GRID_R = 4
GRID_C = 8
REPLICAS = 16
TOKENS = 3072
NBR = 8
NBC = 14
NBT = 112
CAP = 48


def draw_block_mask(key, part):
    key_full, key_counts, key_perm = jax.random.split(jax.random.fold_in(key, 17), 3)
    tile_count = GRID_R * GRID_C
    counts = jax.random.randint(key_counts, (tile_count,), CAP // 2, CAP + 1)
    full_tile = jax.random.randint(key_full, (), 0, tile_count)
    counts = jnp.where(jnp.arange(tile_count) == full_tile, CAP, counts).astype(jnp.int32)
    tile_keys = jax.random.split(key_perm, tile_count)

    def one_tile(tile_key, kept_count):
        ordering = jax.random.permutation(tile_key, NBT)
        rank_of = jnp.zeros((NBT,), jnp.int32).at[ordering].set(jnp.arange(NBT, dtype=jnp.int32))
        return (rank_of < kept_count).astype(jnp.int32)
    kept_blocks = jax.vmap(one_tile)(tile_keys, counts)
    kept_blocks = kept_blocks.reshape(GRID_R, GRID_C, NBR, NBC).transpose(0, 2, 1, 3)
    return kept_blocks.reshape(GRID_R * NBR, GRID_C * NBC)


def steps_of(stream_key, extent, cuts, least, largest):
    gain = 1.0
    for axis_at, blocks in cuts:
        steps = jax.random.uniform(jax.random.fold_in(jax.random.fold_in(stream_key, 6), axis_at), (blocks,), jnp.float32, least / len(cuts), largest / len(cuts))
        gain = gain * jnp.repeat(jnp.exp(steps), extent[axis_at] // blocks).reshape((-1,) + (1,) * (len(extent) - 1 - axis_at))
    return gain


def normal_values(rng, shape, scale, limit, cuts=(), kind=jnp.bfloat16):
    factor_of = steps_of(rng, shape, cuts, -0.22, 0.18) if cuts else 1.0
    drawn = jax.random.normal(rng, shape, jnp.float32) * scale * factor_of
    return jnp.minimum(jnp.maximum(drawn, -limit), limit).astype(kind)


def setup_inputs(seed: int = 0) -> dict:
    keys = jax.random.split(jax.random.key(seed), 6)
    layer_input = normal_values(keys[0], (TOKENS, D), 1.0, 6.0, ((0, 128), (1, 4)))
    hidden_grad = normal_values(keys[1], (TOKENS, FF), 1.0, 6.0, ((0, 64), (1, 8)))
    gate_slots = normal_values(keys[2], (GRID_R, GRID_C, CAP, BS, BS), (D // 2) ** -0.5, 0.125, ((0, 4), (1, 8), (2, 16)))
    up_slots = normal_values(keys[3], (GRID_R, GRID_C, CAP, BS, BS), (D // 2) ** -0.5, 0.125, ((0, 4), (1, 8), (2, 16)))
    block_mask = draw_block_mask(jax.random.fold_in(keys[5], 71), 0)
    return {"layer_input": layer_input, "hidden_grad": hidden_grad, "gate_slots": gate_slots, "up_slots": up_slots, "block_mask": block_mask}


def rounded(array_in):
    return lax.optimization_barrier(array_in.astype(jnp.bfloat16)).astype(jnp.float32)

def tile_slots(block_mask):
    tile_mask = block_mask.reshape(GRID_R, NBR, GRID_C, NBC).transpose(0, 2, 1, 3).reshape(GRID_R * GRID_C, NBT)
    before = jnp.cumsum(tile_mask, axis=1) - tile_mask
    tile_ids = jnp.arange(GRID_R * GRID_C, dtype=jnp.int32)[:, None]
    where_slot = (tile_ids * CAP + jnp.where(tile_mask > 0, before, 0)).astype(jnp.int32)
    return (tile_mask, where_slot.reshape(-1))

def dense_weight(slot_blocks, tile_mask, where_slot):
    flat_slots = slot_blocks.reshape(GRID_R * GRID_C * CAP, BS, BS)
    blocks = jnp.take(flat_slots, where_slot, axis=0).reshape(GRID_R * GRID_C, NBT, BS, BS)
    blocks = blocks * tile_mask[:, :, None, None].astype(slot_blocks.dtype)
    blocks = blocks.reshape(GRID_R, GRID_C, NBR, NBC, BS, BS).transpose(0, 2, 4, 1, 3, 5)
    return blocks.reshape(D, FF).astype(jnp.float32)

def pack_grad(dense_grad, tile_mask, where_slot):
    blocks = dense_grad.reshape(GRID_R, NBR, BS, GRID_C, NBC, BS).transpose(0, 3, 1, 4, 2, 5)
    blocks = blocks.reshape(GRID_R * GRID_C, NBT, BS, BS) * tile_mask[:, :, None, None].astype(jnp.float32)
    packed = jnp.zeros((GRID_R * GRID_C * CAP, BS, BS), jnp.float32)
    packed = packed.at[where_slot].add(blocks.reshape(GRID_R * GRID_C * NBT, BS, BS))
    return packed.reshape(GRID_R, GRID_C, CAP, BS, BS)

def reference(layer_input, hidden_grad, gate_slots, up_slots, block_mask):
    highest = lax.Precision.HIGHEST
    tile_mask, where_slot = tile_slots(block_mask)
    gate_weight = dense_weight(gate_slots, tile_mask, where_slot)
    up_weight = dense_weight(up_slots, tile_mask, where_slot)
    inputs = layer_input.astype(jnp.float32)
    upstream = hidden_grad.astype(jnp.float32)
    feat_group = D // GRID_R
    gate = jnp.zeros((TOKENS, FF), jnp.float32)
    up_pre = jnp.zeros((TOKENS, FF), jnp.float32)
    for group_idx in range(GRID_R):
        low_row = group_idx * feat_group
        part_in = inputs[:, low_row:low_row + feat_group]
        gate = gate + rounded(jnp.dot(part_in, gate_weight[low_row:low_row + feat_group], precision=highest))
        up_pre = up_pre + rounded(jnp.dot(part_in, up_weight[low_row:low_row + feat_group], precision=highest))
    sigmoid_gate = jax.nn.sigmoid(gate)
    gate_grad = (upstream * up_pre * sigmoid_gate * (1.0 + gate * (1.0 - sigmoid_gate))).astype(jnp.bfloat16)
    up_grad = (upstream * gate * sigmoid_gate).astype(jnp.bfloat16)
    gate_gradf = gate_grad.astype(jnp.float32)
    up_gradf = up_grad.astype(jnp.float32)
    unit_group = FF // GRID_C
    input_sum = jnp.zeros((TOKENS, D), jnp.float32)
    for group_idx in range(GRID_C):
        low_col = group_idx * unit_group
        term = jnp.dot(gate_gradf[:, low_col:low_col + unit_group], gate_weight[:, low_col:low_col + unit_group].T, precision=highest)
        term = term + jnp.dot(up_gradf[:, low_col:low_col + unit_group], up_weight[:, low_col:low_col + unit_group].T, precision=highest)
        input_sum = input_sum + rounded(term)

    def add_replica(accum, replica_items):
        block_in, block_gate, block_up = replica_items
        next_gate = accum[0] + rounded(jnp.dot(block_in.T, block_gate, precision=highest))
        next_up = accum[1] + rounded(jnp.dot(block_in.T, block_up, precision=highest))
        return ((next_gate, next_up), None)
    zero_dense = jnp.zeros((D, FF), jnp.float32)
    replica_items = (inputs.reshape(REPLICAS, TOK, D), gate_gradf.reshape(REPLICAS, TOK, FF), up_gradf.reshape(REPLICAS, TOK, FF))
    (gate_acc, up_acc), unused = lax.scan(add_replica, (zero_dense, zero_dense), replica_items)
    gate_slot_grad = pack_grad(gate_acc / REPLICAS, tile_mask, where_slot)
    up_slot_grad = pack_grad(up_acc / REPLICAS, tile_mask, where_slot)
    return (input_sum.astype(jnp.bfloat16), gate_slot_grad, up_slot_grad)
```

```python
import jax
import jax.numpy as jnp
from jax import lax
from jax.sharding import PartitionSpec as P

F32 = jnp.float32
BF16 = jnp.bfloat16


def _shift(x, axis, n, step):
    return lax.ppermute(x, axis, perm=[(i, (i + step) % n) for i in range(n)])


def ring_gather(x, axis, n):
    ahead = n // 2
    behind = n - 1 - ahead
    out = [None] * n
    out[0] = x
    fwd = x
    bwd = x
    for s in range(1, ahead + 1):
        fwd = _shift(fwd, axis, n, 1)
        out[(n - s) % n] = fwd
        if s <= behind:
            bwd = _shift(bwd, axis, n, -1)
            out[s] = bwd
    return out


def ring_sum_scatter(parts, axis, n):
    ahead = n // 2
    behind = n - 1 - ahead
    fwd = parts[ahead]
    bwd = parts[(n - behind) % n] if behind > 0 else None
    for s in range(1, ahead + 1):
        fwd = _shift(fwd, axis, n, 1)
        total = fwd.astype(F32) + parts[ahead - s].astype(F32)
        fwd = total.astype(BF16) if s < ahead else total
        if s <= behind:
            bwd = _shift(bwd, axis, n, -1)
            if s < behind:
                bwd = (bwd.astype(F32) + parts[(s - behind) % n].astype(F32)).astype(BF16)
    if bwd is None:
        return fwd
    return fwd + bwd.astype(F32)


def on_device(layer_input, hidden_grad, gate_slots, up_slots, block_mask):
    n_dp = lax.axis_size("dp")
    n_row = lax.axis_size("row")
    n_col = lax.axis_size("col")
    k_dp = lax.axis_index("dp")
    k_row = lax.axis_index("row")
    k_col = lax.axis_index("col")
    bs = gate_slots.shape[-1]
    per_dev = gate_slots.shape[2]
    cap = per_dev * n_dp
    feat = layer_input.shape[1]
    units = hidden_grad.shape[1]
    tile_rows = feat // bs
    tile_cols = units // bs
    tok = layer_input.shape[0] * n_col
    rows_per = tok // n_row
    cols_per = tok // n_col

    pair_local = jnp.concatenate([gate_slots[0, 0], up_slots[0, 0]], axis=2)
    pair_rel = jnp.concatenate(ring_gather(pair_local, "dp", n_dp), axis=0)

    x_rel = jnp.stack(ring_gather(layer_input, "col", n_col))
    x_abs = jnp.roll(x_rel, k_col, axis=0).reshape(tok, tile_rows, bs)

    tile_mask = lax.dynamic_slice(
        block_mask, (k_row * tile_rows, k_col * tile_cols), (tile_rows, tile_cols)
    ).reshape(tile_rows * tile_cols)
    kept = tile_mask > 0
    position = jnp.cumsum(kept.astype(jnp.int32)) - 1
    q = jnp.arange(cap, dtype=jnp.int32)
    slot_of_q = ((k_dp + q // per_dev) % n_dp) * per_dev + q % per_dev
    onehot = (kept[None, :] & (position[None, :] == slot_of_q[:, None])).astype(BF16)

    dense = jnp.einsum("qb,qkn->bkn", onehot, pair_rel, preferred_element_type=F32).astype(BF16)
    dense4 = dense.reshape(tile_rows, tile_cols, bs, 2 * bs)

    pre = jnp.einsum("trk,rckn->tcn", x_abs, dense4, preferred_element_type=F32).astype(BF16)
    pre_roll = jnp.roll(pre.reshape(n_row, rows_per, tile_cols, 2 * bs), -k_row, axis=0)
    pre_sum = ring_sum_scatter([pre_roll[m] for m in range(n_row)], "row", n_row)
    gate = pre_sum[..., :bs]
    up = pre_sum[..., bs:]
    upstream = hidden_grad.astype(F32).reshape(rows_per, tile_cols, bs)
    sig = jax.nn.sigmoid(gate)
    gate_grad = (upstream * up * sig * (1.0 + gate * (1.0 - sig))).astype(BF16)
    up_grad = (upstream * gate * sig).astype(BF16)
    grad_local = jnp.concatenate([gate_grad, up_grad], axis=2)
    grad_rel = jnp.stack(ring_gather(grad_local, "row", n_row))
    grad_abs = jnp.roll(grad_rel, k_row, axis=0).reshape(tok, tile_cols, 2 * bs)

    dx = jnp.einsum("tcn,rckn->trk", grad_abs, dense4, preferred_element_type=F32).astype(BF16)
    dx_roll = jnp.roll(dx.reshape(n_col, cols_per, feat), -k_col, axis=0)
    input_grad = ring_sum_scatter([dx_roll[m] for m in range(n_col)], "col", n_col).astype(BF16)

    dw = jnp.einsum("trk,tcn->rckn", x_abs, grad_abs, preferred_element_type=F32).astype(BF16)
    slot_dw = jnp.einsum(
        "qb,bkn->qkn",
        onehot,
        dw.reshape(tile_rows * tile_cols, bs, 2 * bs),
        preferred_element_type=F32,
    ).astype(BF16)
    dw_sum = ring_sum_scatter(
        [slot_dw[m * per_dev:(m + 1) * per_dev] for m in range(n_dp)], "dp", n_dp
    ) / n_dp
    gate_out = dw_sum[..., :bs][None, None]
    up_out = dw_sum[..., bs:][None, None]
    return (input_grad, gate_out, up_out)


def solution(mesh):
    return jax.shard_map(
        on_device,
        mesh=mesh,
        in_specs=(
            P(("dp", "col"), "row"),
            P(("dp", "row"), "col"),
            P("row", "col", "dp", None, None),
            P("row", "col", "dp", None, None),
            P(),
        ),
        out_specs=(
            P(("dp", "col"), "row"),
            P("row", "col", "dp", None, None),
            P("row", "col", "dp", None, None),
        ),
        check_vma=False,
    )
```

```python
import jax
import jax.numpy as jnp
from jax import lax
from jax.sharding import PartitionSpec as P

F32 = jnp.float32
BF16 = jnp.bfloat16


def _shift(x, axis, n, step):
    return lax.ppermute(x, axis, perm=[(i, (i + step) % n) for i in range(n)])


def ring_gather(x, axis, n):
    ahead = n // 2
    behind = n - 1 - ahead
    out = [None] * n
    out[0] = x
    fwd = x
    bwd = x
    for s in range(1, ahead + 1):
        fwd = _shift(fwd, axis, n, 1)
        out[(n - s) % n] = fwd
        if s <= behind:
            bwd = _shift(bwd, axis, n, -1)
            out[s] = bwd
    return out


def ring_sum_scatter(parts, axis, n):
    ahead = n // 2
    behind = n - 1 - ahead
    fwd = parts[ahead]
    bwd = parts[(n - behind) % n] if behind > 0 else None
    for s in range(1, ahead + 1):
        fwd = _shift(fwd, axis, n, 1)
        total = fwd.astype(F32) + parts[ahead - s].astype(F32)
        fwd = total.astype(BF16) if s < ahead else total
        if s <= behind:
            bwd = _shift(bwd, axis, n, -1)
            if s < behind:
                bwd = (bwd.astype(F32) + parts[(s - behind) % n].astype(F32)).astype(BF16)
    if bwd is None:
        return fwd
    return fwd + bwd.astype(F32)


def on_device(layer_input, hidden_grad, gate_slots, up_slots, block_mask):
    n_dp = lax.axis_size("dp")
    n_row = lax.axis_size("row")
    n_col = lax.axis_size("col")
    k_dp = lax.axis_index("dp")
    k_row = lax.axis_index("row")
    k_col = lax.axis_index("col")
    bs = gate_slots.shape[-1]
    per_dev = gate_slots.shape[2]
    cap = per_dev * n_dp
    feat = layer_input.shape[1]
    units = hidden_grad.shape[1]
    tile_rows = feat // bs
    tile_cols = units // bs
    tok = layer_input.shape[0] * n_col
    rows_per = tok // n_row
    cols_per = tok // n_col

    pair_local = jnp.concatenate([gate_slots[0, 0], up_slots[0, 0]], axis=2)
    pair_local = pair_local.reshape(per_dev * bs, 2 * bs)
    pair_rel = jnp.concatenate(ring_gather(pair_local, "dp", n_dp), axis=0)
    pair_rel = pair_rel.reshape(cap, bs, 2 * bs)

    x_rel = jnp.stack(ring_gather(layer_input, "col", n_col))
    x_abs = jnp.roll(x_rel, k_col, axis=0).reshape(tok, feat)

    tile_mask = lax.dynamic_slice(
        block_mask, (k_row * tile_rows, k_col * tile_cols), (tile_rows, tile_cols)
    ).reshape(tile_rows * tile_cols)
    kept = tile_mask > 0
    position = jnp.cumsum(kept.astype(jnp.int32)) - 1
    q = jnp.arange(cap, dtype=jnp.int32)
    slot_rel = ((k_dp + q // per_dev) % n_dp) * per_dev + q % per_dev
    onehot_rel = (kept[None, :] & (position[None, :] == slot_rel[:, None])).astype(BF16)
    onehot_abs = (kept[None, :] & (position[None, :] == q[:, None])).astype(BF16)

    dense = jnp.einsum("qb,qkn->bkn", onehot_rel, pair_rel, preferred_element_type=F32).astype(BF16)
    wd = dense.reshape(tile_rows, tile_cols, bs, 2 * bs).transpose(0, 2, 1, 3)
    wd = wd.reshape(feat, tile_cols * 2 * bs)

    pre = jnp.dot(x_abs, wd, preferred_element_type=F32).astype(BF16)
    pre_roll = jnp.roll(pre.reshape(n_row, rows_per, tile_cols * 2 * bs), -k_row, axis=0)
    pre_sum = ring_sum_scatter([pre_roll[m] for m in range(n_row)], "row", n_row)
    pre_sum = pre_sum.reshape(rows_per, tile_cols, 2 * bs)
    gate = pre_sum[..., :bs]
    up = pre_sum[..., bs:]
    upstream = hidden_grad.astype(F32).reshape(rows_per, tile_cols, bs)
    sig = jax.nn.sigmoid(gate)
    gate_grad = (upstream * up * sig * (1.0 + gate * (1.0 - sig))).astype(BF16)
    up_grad = (upstream * gate * sig).astype(BF16)
    grad_local = jnp.concatenate([gate_grad, up_grad], axis=2).reshape(rows_per, tile_cols * 2 * bs)
    grad_rel = jnp.stack(ring_gather(grad_local, "row", n_row))
    grad_abs = jnp.roll(grad_rel, k_row, axis=0).reshape(tok, tile_cols * 2 * bs)

    dx = lax.dot_general(
        grad_abs, wd, (((1,), (1,)), ((), ())), preferred_element_type=F32
    ).astype(BF16)
    dx_roll = jnp.roll(dx.reshape(n_col, cols_per, feat), -k_col, axis=0)
    input_grad = ring_sum_scatter([dx_roll[m] for m in range(n_col)], "col", n_col).astype(BF16)

    dw = lax.dot_general(
        x_abs, grad_abs, (((0,), (0,)), ((), ())), preferred_element_type=F32
    ).astype(BF16)
    dw_blocks = dw.reshape(tile_rows, bs, tile_cols, 2 * bs).transpose(0, 2, 1, 3)
    dw_blocks = dw_blocks.reshape(tile_rows * tile_cols, bs, 2 * bs)
    slot_dw = jnp.einsum("qb,bkn->qkn", onehot_abs, dw_blocks, preferred_element_type=F32).astype(BF16)
    dw_sum = lax.psum_scatter(
        slot_dw.reshape(cap * bs, 2 * bs), "dp", scatter_dimension=0, tiled=True
    ).astype(F32) / n_dp
    dw_sum = dw_sum.reshape(per_dev, bs, 2 * bs)
    gate_out = dw_sum[..., :bs][None, None]
    up_out = dw_sum[..., bs:][None, None]
    return (input_grad, gate_out, up_out)


def solution(mesh):
    return jax.shard_map(
        on_device,
        mesh=mesh,
        in_specs=(
            P(("dp", "col"), "row"),
            P(("dp", "row"), "col"),
            P("row", "col", "dp", None, None),
            P("row", "col", "dp", None, None),
            P(),
        ),
        out_specs=(
            P(("dp", "col"), "row"),
            P("row", "col", "dp", None, None),
            P("row", "col", "dp", None, None),
        ),
        check_vma=False,
    )
```

```python
import jax
import jax.numpy as jnp
from jax import lax
from jax.sharding import PartitionSpec as P

F32 = jnp.float32
BF16 = jnp.bfloat16


def _shift(x, axis, n, step):
    return lax.ppermute(x, axis, perm=[(i, (i + step) % n) for i in range(n)])


def ring_gather(x, axis, n):
    ahead = n // 2
    behind = n - 1 - ahead
    out = [None] * n
    out[0] = x
    fwd = x
    bwd = x
    for s in range(1, ahead + 1):
        fwd = _shift(fwd, axis, n, 1)
        out[(n - s) % n] = fwd
        if s <= behind:
            bwd = _shift(bwd, axis, n, -1)
            out[s] = bwd
    return out


def ring_sum_scatter(parts, axis, n):
    ahead = n // 2
    behind = n - 1 - ahead
    fwd = parts[ahead]
    bwd = parts[(n - behind) % n] if behind > 0 else None
    for s in range(1, ahead + 1):
        fwd = _shift(fwd, axis, n, 1)
        total = fwd.astype(F32) + parts[ahead - s].astype(F32)
        fwd = total.astype(BF16) if s < ahead else total
        if s <= behind:
            bwd = _shift(bwd, axis, n, -1)
            if s < behind:
                bwd = (bwd.astype(F32) + parts[(s - behind) % n].astype(F32)).astype(BF16)
    if bwd is None:
        return fwd
    return fwd + bwd.astype(F32)


def on_device(layer_input, hidden_grad, gate_slots, up_slots, block_mask):
    n_dp = lax.axis_size("dp")
    n_row = lax.axis_size("row")
    n_col = lax.axis_size("col")
    k_dp = lax.axis_index("dp")
    k_row = lax.axis_index("row")
    k_col = lax.axis_index("col")
    bs = gate_slots.shape[-1]
    per_dev = gate_slots.shape[2]
    cap = per_dev * n_dp
    feat = layer_input.shape[1]
    units = hidden_grad.shape[1]
    tile_rows = feat // bs
    tile_cols = units // bs
    tok = layer_input.shape[0] * n_col
    rows_per = tok // n_row
    cols_per = tok // n_col

    pair_local = jnp.concatenate([gate_slots[0, 0], up_slots[0, 0]], axis=2)
    pair_local = pair_local.reshape(per_dev * bs, 2 * bs)
    pair_all = lax.all_gather(pair_local, "dp", axis=0, tiled=True).reshape(cap, bs, 2 * bs)

    x_rel = jnp.stack(ring_gather(layer_input, "col", n_col))
    x_abs = jnp.roll(x_rel, k_col, axis=0).reshape(tok, feat)

    tile_mask = lax.dynamic_slice(
        block_mask, (k_row * tile_rows, k_col * tile_cols), (tile_rows, tile_cols)
    ).reshape(tile_rows * tile_cols)
    kept = tile_mask > 0
    position = jnp.cumsum(kept.astype(jnp.int32)) - 1
    q = jnp.arange(cap, dtype=jnp.int32)
    picks = kept[None, :] & (position[None, :] == q[:, None])
    onehot = picks.astype(BF16)
    onehot3 = onehot.reshape(cap, tile_rows, tile_cols)
    row_pick = jnp.sum(onehot3, axis=2)
    col_pick = jnp.sum(onehot3, axis=1)

    dense = jnp.einsum("qb,qkn->bkn", onehot, pair_all, preferred_element_type=F32).astype(BF16)
    wd = dense.reshape(tile_rows, tile_cols, bs, 2 * bs).transpose(0, 2, 1, 3)
    wd = wd.reshape(feat, tile_cols * 2 * bs)

    pre = jnp.dot(x_abs, wd, preferred_element_type=F32).astype(BF16)
    pre_roll = jnp.roll(pre.reshape(n_row, rows_per, tile_cols * 2 * bs), -k_row, axis=0)
    pre_sum = ring_sum_scatter([pre_roll[m] for m in range(n_row)], "row", n_row)
    pre_sum = pre_sum.reshape(rows_per, tile_cols, 2 * bs)
    gate = pre_sum[..., :bs]
    up = pre_sum[..., bs:]
    upstream = hidden_grad.astype(F32).reshape(rows_per, tile_cols, bs)
    sig = jax.nn.sigmoid(gate)
    gate_grad = (upstream * up * sig * (1.0 + gate * (1.0 - sig))).astype(BF16)
    up_grad = (upstream * gate * sig).astype(BF16)
    grad_local = jnp.concatenate([gate_grad, up_grad], axis=2).reshape(rows_per, tile_cols * 2 * bs)
    grad_rel = jnp.stack(ring_gather(grad_local, "row", n_row))
    grad_abs = jnp.roll(grad_rel, k_row, axis=0).reshape(tok, tile_cols * 2 * bs)

    dx = lax.dot_general(
        grad_abs, wd, (((1,), (1,)), ((), ())), preferred_element_type=F32
    ).astype(BF16)
    dx_roll = jnp.roll(dx.reshape(n_col, cols_per, feat), -k_col, axis=0)
    input_grad = ring_sum_scatter([dx_roll[m] for m in range(n_col)], "col", n_col).astype(BF16)

    x_pick = jnp.einsum(
        "qr,trk->qtk", row_pick, x_abs.reshape(tok, tile_rows, bs), preferred_element_type=F32
    ).astype(BF16)
    g_pick = jnp.einsum(
        "qc,tcn->qtn", col_pick, grad_abs.reshape(tok, tile_cols, 2 * bs), preferred_element_type=F32
    ).astype(BF16)
    slot_dw = jnp.einsum("qtk,qtn->qkn", x_pick, g_pick, preferred_element_type=F32).astype(BF16)
    dw_sum = lax.psum_scatter(
        slot_dw.reshape(cap * bs, 2 * bs), "dp", scatter_dimension=0, tiled=True
    ).astype(F32) / n_dp
    dw_sum = dw_sum.reshape(per_dev, bs, 2 * bs)
    gate_out = dw_sum[..., :bs][None, None]
    up_out = dw_sum[..., bs:][None, None]
    return (input_grad, gate_out, up_out)


def solution(mesh):
    return jax.shard_map(
        on_device,
        mesh=mesh,
        in_specs=(
            P(("dp", "col"), "row"),
            P(("dp", "row"), "col"),
            P("row", "col", "dp", None, None),
            P("row", "col", "dp", None, None),
            P(),
        ),
        out_specs=(
            P(("dp", "col"), "row"),
            P("row", "col", "dp", None, None),
            P("row", "col", "dp", None, None),
        ),
        check_vma=False,
    )
```

```python
import jax
import jax.numpy as jnp
from jax import lax
from jax.sharding import PartitionSpec as P

F32 = jnp.float32
BF16 = jnp.bfloat16


def _shift(x, axis, n, step):
    return lax.ppermute(x, axis, perm=[(i, (i + step) % n) for i in range(n)])


def ring_gather(x, axis, n):
    ahead = n // 2
    behind = n - 1 - ahead
    out = [None] * n
    out[0] = x
    fwd = x
    bwd = x
    for s in range(1, ahead + 1):
        fwd = _shift(fwd, axis, n, 1)
        out[(n - s) % n] = fwd
        if s <= behind:
            bwd = _shift(bwd, axis, n, -1)
            out[s] = bwd
    return out


def ring_sum_scatter(parts, axis, n):
    ahead = n // 2
    behind = n - 1 - ahead
    fwd = parts[ahead]
    bwd = parts[(n - behind) % n] if behind > 0 else None
    for s in range(1, ahead + 1):
        fwd = _shift(fwd, axis, n, 1)
        total = fwd.astype(F32) + parts[ahead - s].astype(F32)
        fwd = total.astype(BF16) if s < ahead else total
        if s <= behind:
            bwd = _shift(bwd, axis, n, -1)
            if s < behind:
                bwd = (bwd.astype(F32) + parts[(s - behind) % n].astype(F32)).astype(BF16)
    if bwd is None:
        return fwd
    return fwd + bwd.astype(F32)


def on_device(layer_input, hidden_grad, gate_slots, up_slots, block_mask):
    n_dp = lax.axis_size("dp")
    n_row = lax.axis_size("row")
    n_col = lax.axis_size("col")
    k_dp = lax.axis_index("dp")
    k_row = lax.axis_index("row")
    k_col = lax.axis_index("col")
    bs = gate_slots.shape[-1]
    per_dev = gate_slots.shape[2]
    cap = per_dev * n_dp
    feat = layer_input.shape[1]
    units = hidden_grad.shape[1]
    tile_rows = feat // bs
    tile_cols = units // bs
    tok = layer_input.shape[0] * n_col
    rows_per = tok // n_row
    cols_per = tok // n_col

    pair_local = jnp.concatenate([gate_slots[0, 0], up_slots[0, 0]], axis=2)
    pair_local = pair_local.reshape(per_dev * bs, 2 * bs)
    pair_all = lax.all_gather(pair_local, "dp", axis=0, tiled=True).reshape(cap, bs, 2 * bs)

    x_rel = jnp.stack(ring_gather(layer_input, "col", n_col))
    x_abs = jnp.roll(x_rel, k_col, axis=0).reshape(tok, tile_rows, bs)

    tile_mask = lax.dynamic_slice(
        block_mask, (k_row * tile_rows, k_col * tile_cols), (tile_rows, tile_cols)
    ).reshape(tile_rows * tile_cols)
    kept = tile_mask > 0
    position = jnp.cumsum(kept.astype(jnp.int32)) - 1
    q = jnp.arange(cap, dtype=jnp.int32)
    picks = kept[None, :] & (position[None, :] == q[:, None])
    onehot3 = picks.astype(BF16).reshape(cap, tile_rows, tile_cols)
    row_pick = jnp.sum(onehot3, axis=2)
    col_pick = jnp.sum(onehot3, axis=1)
    highest = lax.Precision.HIGHEST

    x_pick = jnp.einsum("qr,trk->qtk", row_pick, x_abs, preferred_element_type=F32).astype(BF16)
    per_slot = jnp.einsum("qtk,qkn->qtn", x_pick, pair_all, preferred_element_type=F32)
    pre = jnp.einsum(
        "qc,qtn->ctn", col_pick.astype(F32), per_slot, precision=highest, preferred_element_type=F32
    ).astype(BF16)
    pre_roll = jnp.roll(pre.reshape(tile_cols, n_row, rows_per, 2 * bs), -k_row, axis=1)
    pre_sum = ring_sum_scatter([pre_roll[:, m] for m in range(n_row)], "row", n_row)
    gate = pre_sum[..., :bs]
    up = pre_sum[..., bs:]
    upstream = hidden_grad.astype(F32).reshape(rows_per, tile_cols, bs).transpose(1, 0, 2)
    sig = jax.nn.sigmoid(gate)
    gate_grad = (upstream * up * sig * (1.0 + gate * (1.0 - sig))).astype(BF16)
    up_grad = (upstream * gate * sig).astype(BF16)
    grad_local = jnp.concatenate([gate_grad, up_grad], axis=2)
    grad_rel = jnp.stack(ring_gather(grad_local, "row", n_row), axis=1)
    grad_abs = jnp.roll(grad_rel, k_row, axis=1).reshape(tile_cols, tok, 2 * bs)

    g_pick = jnp.einsum("qc,ctn->qtn", col_pick, grad_abs, preferred_element_type=F32).astype(BF16)
    slot_dw = jnp.einsum("qtk,qtn->qkn", x_pick, g_pick, preferred_element_type=F32).astype(BF16)

    dx_slot = jnp.einsum("qtn,qkn->qtk", g_pick, pair_all, preferred_element_type=F32)
    dx = jnp.einsum(
        "qr,qtk->rtk", row_pick.astype(F32), dx_slot, precision=highest, preferred_element_type=F32
    ).astype(BF16)
    dx_roll = jnp.roll(dx.reshape(tile_rows, n_col, cols_per, bs), -k_col, axis=1)
    dx_sum = ring_sum_scatter([dx_roll[:, m] for m in range(n_col)], "col", n_col)
    input_grad = dx_sum.transpose(1, 0, 2).reshape(cols_per, feat).astype(BF16)

    dw_sum = lax.psum_scatter(
        slot_dw.reshape(cap * bs, 2 * bs), "dp", scatter_dimension=0, tiled=True
    ).astype(F32) / n_dp
    dw_sum = dw_sum.reshape(per_dev, bs, 2 * bs)
    gate_out = dw_sum[..., :bs][None, None]
    up_out = dw_sum[..., bs:][None, None]
    return (input_grad, gate_out, up_out)


def solution(mesh):
    return jax.shard_map(
        on_device,
        mesh=mesh,
        in_specs=(
            P(("dp", "col"), "row"),
            P(("dp", "row"), "col"),
            P("row", "col", "dp", None, None),
            P("row", "col", "dp", None, None),
            P(),
        ),
        out_specs=(
            P(("dp", "col"), "row"),
            P("row", "col", "dp", None, None),
            P("row", "col", "dp", None, None),
        ),
        check_vma=False,
    )
```

```python
import jax
import jax.numpy as jnp
from jax import lax
from jax.sharding import PartitionSpec as P

F32 = jnp.float32
BF16 = jnp.bfloat16


def _shift(x, axis, n, step):
    return lax.ppermute(x, axis, perm=[(i, (i + step) % n) for i in range(n)])


def ring_gather(x, axis, n):
    ahead = n // 2
    behind = n - 1 - ahead
    out = [None] * n
    out[0] = x
    fwd = x
    bwd = x
    for s in range(1, ahead + 1):
        fwd = _shift(fwd, axis, n, 1)
        out[(n - s) % n] = fwd
        if s <= behind:
            bwd = _shift(bwd, axis, n, -1)
            out[s] = bwd
    return out


def ring_sum_scatter(parts, axis, n):
    ahead = n // 2
    behind = n - 1 - ahead
    fwd = parts[ahead]
    bwd = parts[(n - behind) % n] if behind > 0 else None
    for s in range(1, ahead + 1):
        fwd = _shift(fwd, axis, n, 1)
        total = fwd.astype(F32) + parts[ahead - s].astype(F32)
        fwd = total.astype(BF16) if s < ahead else total
        if s <= behind:
            bwd = _shift(bwd, axis, n, -1)
            if s < behind:
                bwd = (bwd.astype(F32) + parts[(s - behind) % n].astype(F32)).astype(BF16)
    if bwd is None:
        return fwd
    return fwd + bwd.astype(F32)


def on_device(layer_input, hidden_grad, gate_slots, up_slots, block_mask):
    n_dp = lax.axis_size("dp")
    n_row = lax.axis_size("row")
    n_col = lax.axis_size("col")
    k_dp = lax.axis_index("dp")
    k_row = lax.axis_index("row")
    k_col = lax.axis_index("col")
    bs = gate_slots.shape[-1]
    per_dev = gate_slots.shape[2]
    cap = per_dev * n_dp
    feat = layer_input.shape[1]
    units = hidden_grad.shape[1]
    tile_rows = feat // bs
    tile_cols = units // bs
    tok = layer_input.shape[0] * n_col
    rows_per = tok // n_row
    cols_per = tok // n_col

    gate_all = lax.all_gather(
        gate_slots[0, 0].reshape(per_dev * bs, bs), "dp", axis=0, tiled=True
    ).reshape(cap, bs, bs)
    up_all = lax.all_gather(
        up_slots[0, 0].reshape(per_dev * bs, bs), "dp", axis=0, tiled=True
    ).reshape(cap, bs, bs)

    x_rel = jnp.stack(ring_gather(layer_input, "col", n_col))
    x_abs = jnp.roll(x_rel, k_col, axis=0).reshape(tok, tile_rows, bs)

    tile_mask = lax.dynamic_slice(
        block_mask, (k_row * tile_rows, k_col * tile_cols), (tile_rows, tile_cols)
    ).reshape(tile_rows * tile_cols)
    kept = tile_mask > 0
    position = jnp.cumsum(kept.astype(jnp.int32)) - 1
    q = jnp.arange(cap, dtype=jnp.int32)
    picks = kept[None, :] & (position[None, :] == q[:, None])
    onehot3 = picks.astype(BF16).reshape(cap, tile_rows, tile_cols)
    row_pick = jnp.sum(onehot3, axis=2)
    col_pick = jnp.sum(onehot3, axis=1)
    high = lax.Precision.HIGH

    x_pick = jnp.einsum("qr,trk->qtk", row_pick, x_abs, preferred_element_type=F32).astype(BF16)

    def pre_rows(weights):
        per_slot = jnp.einsum("qtk,qkn->qtn", x_pick, weights, preferred_element_type=F32)
        pre = jnp.einsum(
            "qc,qtn->ctn", col_pick.astype(F32), per_slot, precision=high, preferred_element_type=F32
        ).astype(BF16)
        pre_roll = jnp.roll(pre.reshape(tile_cols, n_row, rows_per, bs), -k_row, axis=1)
        return ring_sum_scatter([pre_roll[:, m] for m in range(n_row)], "row", n_row)

    gate = pre_rows(gate_all)
    up = pre_rows(up_all)
    upstream = hidden_grad.astype(F32).reshape(rows_per, tile_cols, bs).transpose(1, 0, 2)
    sig = jax.nn.sigmoid(gate)
    gate_grad = (upstream * up * sig * (1.0 + gate * (1.0 - sig))).astype(BF16)
    up_grad = (upstream * gate * sig).astype(BF16)

    def grad_slots(grad_part):
        grad_rel = jnp.stack(ring_gather(grad_part, "row", n_row), axis=1)
        grad_abs = jnp.roll(grad_rel, k_row, axis=1).reshape(tile_cols, tok, bs)
        return jnp.einsum("qc,ctn->qtn", col_pick, grad_abs, preferred_element_type=F32).astype(BF16)

    def slot_grad(picked):
        slot_dw = jnp.einsum("qtk,qtn->qkn", x_pick, picked, preferred_element_type=F32).astype(BF16)
        total = lax.psum_scatter(slot_dw.reshape(cap * bs, bs), "dp", scatter_dimension=0, tiled=True)
        return (total.astype(F32) / n_dp).reshape(per_dev, bs, bs)[None, None]

    gate_pick = grad_slots(gate_grad)
    gate_out = slot_grad(gate_pick)
    up_pick = grad_slots(up_grad)
    up_out = slot_grad(up_pick)

    dx_slot = jnp.einsum("qtn,qkn->qtk", gate_pick, gate_all, preferred_element_type=F32)
    dx_slot = dx_slot + jnp.einsum("qtn,qkn->qtk", up_pick, up_all, preferred_element_type=F32)
    dx = jnp.einsum(
        "qr,qtk->rtk", row_pick.astype(F32), dx_slot, precision=high, preferred_element_type=F32
    ).astype(BF16)
    dx_roll = jnp.roll(dx.reshape(tile_rows, n_col, cols_per, bs), -k_col, axis=1)
    dx_sum = ring_sum_scatter([dx_roll[:, m] for m in range(n_col)], "col", n_col)
    input_grad = dx_sum.transpose(1, 0, 2).reshape(cols_per, feat).astype(BF16)
    return (input_grad, gate_out, up_out)


def solution(mesh):
    return jax.shard_map(
        on_device,
        mesh=mesh,
        in_specs=(
            P(("dp", "col"), "row"),
            P(("dp", "row"), "col"),
            P("row", "col", "dp", None, None),
            P("row", "col", "dp", None, None),
            P(),
        ),
        out_specs=(
            P(("dp", "col"), "row"),
            P("row", "col", "dp", None, None),
            P("row", "col", "dp", None, None),
        ),
        check_vma=False,
    )
```

```python
import jax
import jax.numpy as jnp
from jax import lax
from jax.sharding import PartitionSpec as P

F32 = jnp.float32
BF16 = jnp.bfloat16


def _shift(x, axis, n, step):
    return lax.ppermute(x, axis, perm=[(i, (i + step) % n) for i in range(n)])


def ring_gather(x, axis, n):
    ahead = n // 2
    behind = n - 1 - ahead
    out = [None] * n
    out[0] = x
    fwd = x
    bwd = x
    for s in range(1, ahead + 1):
        fwd = _shift(fwd, axis, n, 1)
        out[(n - s) % n] = fwd
        if s <= behind:
            bwd = _shift(bwd, axis, n, -1)
            out[s] = bwd
    return out


def ring_sum_scatter(parts, axis, n):
    ahead = n // 2
    behind = n - 1 - ahead
    fwd = parts[ahead]
    bwd = parts[(n - behind) % n] if behind > 0 else None
    for s in range(1, ahead + 1):
        fwd = _shift(fwd, axis, n, 1)
        total = fwd.astype(F32) + parts[ahead - s].astype(F32)
        fwd = total.astype(BF16) if s < ahead else total
        if s <= behind:
            bwd = _shift(bwd, axis, n, -1)
            if s < behind:
                bwd = (bwd.astype(F32) + parts[(s - behind) % n].astype(F32)).astype(BF16)
    if bwd is None:
        return fwd
    return fwd + bwd.astype(F32)


def _halves(x, half):
    return x[..., :half], x[..., half:]


def ring4_gather(x, axis, half):
    n = 4
    from_left = _shift(x, axis, n, 1)
    from_right = _shift(x, axis, n, -1)
    far_a = _shift(_halves(from_left, half)[0], axis, n, 1)
    far_b = _shift(_halves(from_right, half)[1], axis, n, -1)
    return [x, from_right, jnp.concatenate([far_a, far_b], axis=-1), from_left]


def ring4_sum_scatter(parts, axis, half):
    n = 4
    own_a, own_b = _halves(parts[0], half)
    next_a, next_b = _halves(parts[1], half)
    far_a, far_b = _halves(parts[2], half)
    prev_a, prev_b = _halves(parts[3], half)
    got_left = _shift(jnp.concatenate([far_a, next_b], axis=-1), axis, n, 1)
    got_right = _shift(jnp.concatenate([prev_a, far_b], axis=-1), axis, n, -1)
    left_a, left_b = _halves(got_left, half)
    right_a, right_b = _halves(got_right, half)
    send_a = (left_a.astype(F32) + next_a.astype(F32)).astype(BF16)
    send_b = (right_b.astype(F32) + prev_b.astype(F32)).astype(BF16)
    two_left = _shift(send_a, axis, n, 1)
    two_right = _shift(send_b, axis, n, -1)
    total_a = own_a.astype(F32) + two_left.astype(F32) + right_a.astype(F32)
    total_b = own_b.astype(F32) + two_right.astype(F32) + left_b.astype(F32)
    return jnp.concatenate([total_a, total_b], axis=-1)


def on_device(layer_input, hidden_grad, gate_slots, up_slots, block_mask):
    n_dp = lax.axis_size("dp")
    n_row = lax.axis_size("row")
    n_col = lax.axis_size("col")
    k_dp = lax.axis_index("dp")
    k_row = lax.axis_index("row")
    k_col = lax.axis_index("col")
    bs = gate_slots.shape[-1]
    per_dev = gate_slots.shape[2]
    cap = per_dev * n_dp
    feat = layer_input.shape[1]
    units = hidden_grad.shape[1]
    tile_rows = feat // bs
    tile_cols = units // bs
    tok = layer_input.shape[0] * n_col
    rows_per = tok // n_row
    cols_per = tok // n_col

    pair_local = jnp.concatenate([gate_slots[0, 0], up_slots[0, 0]], axis=2)
    pair_local = pair_local.reshape(per_dev * bs, 2 * bs)
    pair_all = lax.all_gather(pair_local, "dp", axis=0, tiled=True).reshape(cap, bs, 2 * bs)

    x_rel = jnp.stack(ring_gather(layer_input, "col", n_col))
    x_abs = jnp.roll(x_rel, k_col, axis=0).reshape(tok, tile_rows, bs)

    tile_mask = lax.dynamic_slice(
        block_mask, (k_row * tile_rows, k_col * tile_cols), (tile_rows, tile_cols)
    ).reshape(tile_rows * tile_cols)
    kept = tile_mask > 0
    position = jnp.cumsum(kept.astype(jnp.int32)) - 1
    q = jnp.arange(cap, dtype=jnp.int32)
    picks = kept[None, :] & (position[None, :] == q[:, None])
    onehot3 = picks.astype(BF16).reshape(cap, tile_rows, tile_cols)
    row_pick = jnp.sum(onehot3, axis=2)
    col_pick = jnp.sum(onehot3, axis=1)
    highest = lax.Precision.HIGH

    x_pick = jnp.einsum("qr,trk->qtk", row_pick, x_abs, preferred_element_type=F32).astype(BF16)
    per_slot = jnp.einsum("qtk,qkn->qtn", x_pick, pair_all, preferred_element_type=F32)
    pre = jnp.einsum(
        "qc,qtn->ctn", col_pick.astype(F32), per_slot, precision=highest, preferred_element_type=F32
    ).astype(BF16)
    pre_roll = jnp.roll(pre.reshape(tile_cols, n_row, rows_per, 2 * bs), -k_row, axis=1)
    if n_row == 4:
        pre_sum = ring4_sum_scatter([pre_roll[:, m] for m in range(n_row)], "row", bs)
    else:
        pre_sum = ring_sum_scatter([pre_roll[:, m] for m in range(n_row)], "row", n_row)
    gate = pre_sum[..., :bs]
    up = pre_sum[..., bs:]
    upstream = hidden_grad.astype(F32).reshape(rows_per, tile_cols, bs).transpose(1, 0, 2)
    sig = jax.nn.sigmoid(gate)
    gate_grad = (upstream * up * sig * (1.0 + gate * (1.0 - sig))).astype(BF16)
    up_grad = (upstream * gate * sig).astype(BF16)
    grad_local = jnp.concatenate([gate_grad, up_grad], axis=2)
    if n_row == 4:
        grad_rel = jnp.stack(ring4_gather(grad_local, "row", bs), axis=1)
    else:
        grad_rel = jnp.stack(ring_gather(grad_local, "row", n_row), axis=1)
    grad_abs = jnp.roll(grad_rel, k_row, axis=1).reshape(tile_cols, tok, 2 * bs)

    g_pick = jnp.einsum("qc,ctn->qtn", col_pick, grad_abs, preferred_element_type=F32).astype(BF16)
    slot_dw = jnp.einsum("qtk,qtn->qkn", x_pick, g_pick, preferred_element_type=F32).astype(BF16)

    dx_slot = jnp.einsum("qtn,qkn->qtk", g_pick, pair_all, preferred_element_type=F32)
    dx = jnp.einsum(
        "qr,qtk->rtk", row_pick.astype(F32), dx_slot, precision=highest, preferred_element_type=F32
    ).astype(BF16)
    dx_roll = jnp.roll(dx.reshape(tile_rows, n_col, cols_per, bs), -k_col, axis=1)
    dx_sum = ring_sum_scatter([dx_roll[:, m] for m in range(n_col)], "col", n_col)
    input_grad = dx_sum.transpose(1, 0, 2).reshape(cols_per, feat).astype(BF16)

    dw_sum = lax.psum_scatter(
        slot_dw.reshape(cap * bs, 2 * bs), "dp", scatter_dimension=0, tiled=True
    ).astype(F32) / n_dp
    dw_sum = dw_sum.reshape(per_dev, bs, 2 * bs)
    gate_out = dw_sum[..., :bs][None, None]
    up_out = dw_sum[..., bs:][None, None]
    return (input_grad, gate_out, up_out)


def solution(mesh):
    return jax.shard_map(
        on_device,
        mesh=mesh,
        in_specs=(
            P(("dp", "col"), "row"),
            P(("dp", "row"), "col"),
            P("row", "col", "dp", None, None),
            P("row", "col", "dp", None, None),
            P(),
        ),
        out_specs=(
            P(("dp", "col"), "row"),
            P("row", "col", "dp", None, None),
            P("row", "col", "dp", None, None),
        ),
        check_vma=False,
    )
```

```python
import jax
import jax.numpy as jnp
from jax import lax
from jax.sharding import PartitionSpec as P

F32 = jnp.float32
BF16 = jnp.bfloat16


def _shift(x, axis, n, step):
    return lax.ppermute(x, axis, perm=[(i, (i + step) % n) for i in range(n)])


def ring_gather(x, axis, n):
    ahead = n // 2
    behind = n - 1 - ahead
    out = [None] * n
    out[0] = x
    fwd = x
    bwd = x
    for s in range(1, ahead + 1):
        fwd = _shift(fwd, axis, n, 1)
        out[(n - s) % n] = fwd
        if s <= behind:
            bwd = _shift(bwd, axis, n, -1)
            out[s] = bwd
    return out


def ring_sum_scatter(parts, axis, n):
    ahead = n // 2
    behind = n - 1 - ahead
    fwd = parts[ahead]
    bwd = parts[(n - behind) % n] if behind > 0 else None
    for s in range(1, ahead + 1):
        fwd = _shift(fwd, axis, n, 1)
        total = fwd.astype(F32) + parts[ahead - s].astype(F32)
        fwd = total.astype(BF16) if s < ahead else total
        if s <= behind:
            bwd = _shift(bwd, axis, n, -1)
            if s < behind:
                bwd = (bwd.astype(F32) + parts[(s - behind) % n].astype(F32)).astype(BF16)
    if bwd is None:
        return fwd
    return fwd + bwd.astype(F32)


def _halves(x, half):
    return x[..., :half], x[..., half:]


def ring4_gather(x, axis, half):
    n = 4
    from_left = _shift(x, axis, n, 1)
    from_right = _shift(x, axis, n, -1)
    far_a = _shift(_halves(from_left, half)[0], axis, n, 1)
    far_b = _shift(_halves(from_right, half)[1], axis, n, -1)
    return [x, from_right, jnp.concatenate([far_a, far_b], axis=-1), from_left]


def ring4_sum_scatter(parts, axis, half):
    n = 4
    own_a, own_b = _halves(parts[0], half)
    next_a, next_b = _halves(parts[1], half)
    far_a, far_b = _halves(parts[2], half)
    prev_a, prev_b = _halves(parts[3], half)
    got_left = _shift(jnp.concatenate([far_a, next_b], axis=-1), axis, n, 1)
    got_right = _shift(jnp.concatenate([prev_a, far_b], axis=-1), axis, n, -1)
    left_a, left_b = _halves(got_left, half)
    right_a, right_b = _halves(got_right, half)
    send_a = (left_a.astype(F32) + next_a.astype(F32)).astype(BF16)
    send_b = (right_b.astype(F32) + prev_b.astype(F32)).astype(BF16)
    two_left = _shift(send_a, axis, n, 1)
    two_right = _shift(send_b, axis, n, -1)
    total_a = own_a.astype(F32) + two_left.astype(F32) + right_a.astype(F32)
    total_b = own_b.astype(F32) + two_right.astype(F32) + left_b.astype(F32)
    return jnp.concatenate([total_a, total_b], axis=-1)


def on_device(layer_input, hidden_grad, gate_slots, up_slots, block_mask):
    n_dp = lax.axis_size("dp")
    n_row = lax.axis_size("row")
    n_col = lax.axis_size("col")
    k_dp = lax.axis_index("dp")
    k_row = lax.axis_index("row")
    k_col = lax.axis_index("col")
    bs = gate_slots.shape[-1]
    per_dev = gate_slots.shape[2]
    cap = per_dev * n_dp
    feat = layer_input.shape[1]
    units = hidden_grad.shape[1]
    tile_rows = feat // bs
    tile_cols = units // bs
    tok = layer_input.shape[0] * n_col
    rows_per = tok // n_row
    cols_per = tok // n_col

    pair_local = jnp.concatenate([gate_slots[0, 0], up_slots[0, 0]], axis=2)
    pair_local = pair_local.reshape(per_dev * bs, 2 * bs)
    pair_all = lax.all_gather(pair_local, "dp", axis=0, tiled=True).reshape(cap, bs, 2 * bs)

    x_rel = jnp.stack(ring_gather(layer_input, "col", n_col))
    x_abs = jnp.roll(x_rel, k_col, axis=0).reshape(tok, tile_rows, bs)

    tile_mask = lax.dynamic_slice(
        block_mask, (k_row * tile_rows, k_col * tile_cols), (tile_rows, tile_cols)
    ).reshape(tile_rows * tile_cols)
    kept = tile_mask > 0
    position = jnp.cumsum(kept.astype(jnp.int32)) - 1
    q = jnp.arange(cap, dtype=jnp.int32)
    picks = kept[None, :] & (position[None, :] == q[:, None])
    onehot3 = picks.astype(BF16).reshape(cap, tile_rows, tile_cols)
    row_pick = jnp.sum(onehot3, axis=2)
    col_pick = jnp.sum(onehot3, axis=1)
    highest = lax.Precision.HIGH

    x_pick = jnp.einsum("qr,trk->qtk", row_pick, x_abs, preferred_element_type=F32).astype(BF16)
    by_col = jnp.einsum(
        "qcr,qkn->ckrn", onehot3.transpose(0, 2, 1), pair_all, preferred_element_type=F32
    ).astype(BF16).reshape(tile_cols, feat, 2 * bs)
    x_kr = x_abs.transpose(0, 2, 1).reshape(1, tok, feat)
    x_wide = jnp.broadcast_to(x_kr, (tile_cols, tok, feat))
    pre = lax.dot_general(
        x_wide, by_col, (((2,), (1,)), ((0,), (0,))), preferred_element_type=F32
    ).astype(BF16)
    pre_roll = jnp.roll(pre.reshape(tile_cols, n_row, rows_per, 2 * bs), -k_row, axis=1)
    if n_row == 4:
        pre_sum = ring4_sum_scatter([pre_roll[:, m] for m in range(n_row)], "row", bs)
    else:
        pre_sum = ring_sum_scatter([pre_roll[:, m] for m in range(n_row)], "row", n_row)
    gate = pre_sum[..., :bs]
    up = pre_sum[..., bs:]
    upstream = hidden_grad.astype(F32).reshape(rows_per, tile_cols, bs).transpose(1, 0, 2)
    sig = jax.nn.sigmoid(gate)
    gate_grad = (upstream * up * sig * (1.0 + gate * (1.0 - sig))).astype(BF16)
    up_grad = (upstream * gate * sig).astype(BF16)
    grad_local = jnp.concatenate([gate_grad, up_grad], axis=2)
    if n_row == 4:
        grad_rel = jnp.stack(ring4_gather(grad_local, "row", bs), axis=1)
    else:
        grad_rel = jnp.stack(ring_gather(grad_local, "row", n_row), axis=1)
    grad_abs = jnp.roll(grad_rel, k_row, axis=1).reshape(tile_cols, tok, 2 * bs)

    g_pick = jnp.einsum("qc,ctn->qtn", col_pick, grad_abs, preferred_element_type=F32).astype(BF16)
    slot_dw = jnp.einsum("qtk,qtn->qkn", x_pick, g_pick, preferred_element_type=F32).astype(BF16)

    dx_slot = jnp.einsum("qtn,qkn->qtk", g_pick, pair_all, preferred_element_type=F32)
    dx = jnp.einsum(
        "qr,qtk->rtk", row_pick.astype(F32), dx_slot, precision=highest, preferred_element_type=F32
    ).astype(BF16)
    dx_roll = jnp.roll(dx.reshape(tile_rows, n_col, cols_per, bs), -k_col, axis=1)
    dx_sum = ring_sum_scatter([dx_roll[:, m] for m in range(n_col)], "col", n_col)
    input_grad = dx_sum.transpose(1, 0, 2).reshape(cols_per, feat).astype(BF16)

    dw_sum = lax.psum_scatter(
        slot_dw.reshape(cap * bs, 2 * bs), "dp", scatter_dimension=0, tiled=True
    ).astype(F32) / n_dp
    dw_sum = dw_sum.reshape(per_dev, bs, 2 * bs)
    gate_out = dw_sum[..., :bs][None, None]
    up_out = dw_sum[..., bs:][None, None]
    return (input_grad, gate_out, up_out)


def solution(mesh):
    return jax.shard_map(
        on_device,
        mesh=mesh,
        in_specs=(
            P(("dp", "col"), "row"),
            P(("dp", "row"), "col"),
            P("row", "col", "dp", None, None),
            P("row", "col", "dp", None, None),
            P(),
        ),
        out_specs=(
            P(("dp", "col"), "row"),
            P("row", "col", "dp", None, None),
            P("row", "col", "dp", None, None),
        ),
        check_vma=False,
    )
```

```python
import jax
import jax.numpy as jnp
from jax import lax
from jax.sharding import PartitionSpec as P

F32 = jnp.float32
BF16 = jnp.bfloat16


def _shift(x, axis, n, step):
    return lax.ppermute(x, axis, perm=[(i, (i + step) % n) for i in range(n)])


def ring_gather(x, axis, n):
    ahead = n // 2
    behind = n - 1 - ahead
    out = [None] * n
    out[0] = x
    fwd = x
    bwd = x
    for s in range(1, ahead + 1):
        fwd = _shift(fwd, axis, n, 1)
        out[(n - s) % n] = fwd
        if s <= behind:
            bwd = _shift(bwd, axis, n, -1)
            out[s] = bwd
    return out


def ring_sum_scatter(parts, axis, n):
    ahead = n // 2
    behind = n - 1 - ahead
    fwd = parts[ahead]
    bwd = parts[(n - behind) % n] if behind > 0 else None
    for s in range(1, ahead + 1):
        fwd = _shift(fwd, axis, n, 1)
        total = fwd.astype(F32) + parts[ahead - s].astype(F32)
        fwd = total.astype(BF16) if s < ahead else total
        if s <= behind:
            bwd = _shift(bwd, axis, n, -1)
            if s < behind:
                bwd = (bwd.astype(F32) + parts[(s - behind) % n].astype(F32)).astype(BF16)
    if bwd is None:
        return fwd
    return fwd + bwd.astype(F32)


def _halves(x, half):
    return x[..., :half], x[..., half:]


def ring4_gather(x, axis, half):
    n = 4
    from_left = _shift(x, axis, n, 1)
    from_right = _shift(x, axis, n, -1)
    far_a = _shift(_halves(from_left, half)[0], axis, n, 1)
    far_b = _shift(_halves(from_right, half)[1], axis, n, -1)
    return [x, from_right, jnp.concatenate([far_a, far_b], axis=-1), from_left]


def ring4_sum_scatter(parts, axis, half):
    n = 4
    own_a, own_b = _halves(parts[0], half)
    next_a, next_b = _halves(parts[1], half)
    far_a, far_b = _halves(parts[2], half)
    prev_a, prev_b = _halves(parts[3], half)
    got_left = _shift(jnp.concatenate([far_a, next_b], axis=-1), axis, n, 1)
    got_right = _shift(jnp.concatenate([prev_a, far_b], axis=-1), axis, n, -1)
    left_a, left_b = _halves(got_left, half)
    right_a, right_b = _halves(got_right, half)
    send_a = (left_a.astype(F32) + next_a.astype(F32)).astype(BF16)
    send_b = (right_b.astype(F32) + prev_b.astype(F32)).astype(BF16)
    two_left = _shift(send_a, axis, n, 1)
    two_right = _shift(send_b, axis, n, -1)
    total_a = own_a.astype(F32) + two_left.astype(F32) + right_a.astype(F32)
    total_b = own_b.astype(F32) + two_right.astype(F32) + left_b.astype(F32)
    return jnp.concatenate([total_a, total_b], axis=-1)


def on_device(layer_input, hidden_grad, gate_slots, up_slots, block_mask):
    n_dp = lax.axis_size("dp")
    n_row = lax.axis_size("row")
    n_col = lax.axis_size("col")
    k_dp = lax.axis_index("dp")
    k_row = lax.axis_index("row")
    k_col = lax.axis_index("col")
    bs = gate_slots.shape[-1]
    per_dev = gate_slots.shape[2]
    cap = per_dev * n_dp
    feat = layer_input.shape[1]
    units = hidden_grad.shape[1]
    tile_rows = feat // bs
    tile_cols = units // bs
    tok = layer_input.shape[0] * n_col
    rows_per = tok // n_row
    cols_per = tok // n_col

    pair_local = jnp.concatenate([gate_slots[0, 0], up_slots[0, 0]], axis=2)
    pair_local = pair_local.reshape(per_dev * bs, 2 * bs)
    pair_all = lax.all_gather(pair_local, "dp", axis=0, tiled=True).reshape(cap, bs, 2 * bs)

    x_rel = jnp.stack(ring_gather(layer_input, "col", n_col))
    x_abs = jnp.roll(x_rel, k_col, axis=0).reshape(tok, tile_rows, bs)

    tile_mask = lax.dynamic_slice(
        block_mask, (k_row * tile_rows, k_col * tile_cols), (tile_rows, tile_cols)
    ).reshape(tile_rows * tile_cols)
    kept = tile_mask > 0
    position = jnp.cumsum(kept.astype(jnp.int32)) - 1
    q = jnp.arange(cap, dtype=jnp.int32)
    picks = kept[None, :] & (position[None, :] == q[:, None])
    onehot3 = picks.astype(BF16).reshape(cap, tile_rows, tile_cols)
    row_pick = jnp.sum(onehot3, axis=2)
    col_pick = jnp.sum(onehot3, axis=1)
    highest = lax.Precision.HIGH

    x_pick = jnp.einsum("qr,trk->qtk", row_pick, x_abs, preferred_element_type=F32).astype(BF16)
    by_col = jnp.einsum(
        "qcr,qkn->ckrn", onehot3.transpose(0, 2, 1), pair_all, preferred_element_type=F32
    ).astype(BF16).reshape(tile_cols, feat, 2 * bs)
    x_kr = x_abs.transpose(0, 2, 1).reshape(1, tok, feat)
    x_wide = jnp.broadcast_to(x_kr, (tile_cols, tok, feat))
    pre = lax.dot_general(
        x_wide, by_col, (((2,), (1,)), ((0,), (0,))), preferred_element_type=F32
    ).astype(BF16)
    pre_roll = jnp.roll(pre.reshape(tile_cols, n_row, rows_per, 2 * bs), -k_row, axis=1)
    if n_row == 4:
        pre_sum = ring4_sum_scatter([pre_roll[:, m] for m in range(n_row)], "row", bs)
    else:
        pre_sum = ring_sum_scatter([pre_roll[:, m] for m in range(n_row)], "row", n_row)
    gate = pre_sum[..., :bs]
    up = pre_sum[..., bs:]
    upstream = hidden_grad.astype(F32).reshape(rows_per, tile_cols, bs).transpose(1, 0, 2)
    sig = jax.nn.sigmoid(gate)
    gate_grad = (upstream * up * sig * (1.0 + gate * (1.0 - sig))).astype(BF16)
    up_grad = (upstream * gate * sig).astype(BF16)
    grad_local = jnp.concatenate([gate_grad, up_grad], axis=2)
    if n_row == 4:
        grad_parts = ring4_gather(grad_local, "row", bs)
    else:
        grad_parts = ring_gather(grad_local, "row", n_row)
    x_pick_rel = jnp.roll(x_pick.reshape(cap, n_row, rows_per, bs), -k_row, axis=1)
    pick_parts = [
        jnp.einsum("qc,ctn->qtn", col_pick, part, preferred_element_type=F32).astype(BF16)
        for part in grad_parts
    ]
    dw_total = None
    for m in range(n_row):
        term = jnp.einsum("qtk,qtn->qkn", x_pick_rel[:, m], pick_parts[m], preferred_element_type=F32)
        dw_total = term if dw_total is None else dw_total + term
    slot_dw = dw_total.astype(BF16)
    g_pick = jnp.roll(jnp.stack(pick_parts, axis=1), k_row, axis=1).reshape(cap, tok, 2 * bs)

    dx_slot = jnp.einsum("qtn,qkn->qtk", g_pick, pair_all, preferred_element_type=F32)
    dx = jnp.einsum(
        "qr,qtk->rtk", row_pick.astype(F32), dx_slot, precision=highest, preferred_element_type=F32
    ).astype(BF16)
    dx_roll = jnp.roll(dx.reshape(tile_rows, n_col, cols_per, bs), -k_col, axis=1)
    dx_sum = ring_sum_scatter([dx_roll[:, m] for m in range(n_col)], "col", n_col)
    input_grad = dx_sum.transpose(1, 0, 2).reshape(cols_per, feat).astype(BF16)

    dw_sum = lax.psum_scatter(
        slot_dw.reshape(cap * bs, 2 * bs), "dp", scatter_dimension=0, tiled=True
    ).astype(F32) / n_dp
    dw_sum = dw_sum.reshape(per_dev, bs, 2 * bs)
    gate_out = dw_sum[..., :bs][None, None]
    up_out = dw_sum[..., bs:][None, None]
    return (input_grad, gate_out, up_out)


def solution(mesh):
    return jax.shard_map(
        on_device,
        mesh=mesh,
        in_specs=(
            P(("dp", "col"), "row"),
            P(("dp", "row"), "col"),
            P("row", "col", "dp", None, None),
            P("row", "col", "dp", None, None),
            P(),
        ),
        out_specs=(
            P(("dp", "col"), "row"),
            P("row", "col", "dp", None, None),
            P("row", "col", "dp", None, None),
        ),
        check_vma=False,
    )
```

```python
import jax
import jax.numpy as jnp
from jax import lax
from jax.sharding import PartitionSpec as P

F32 = jnp.float32
BF16 = jnp.bfloat16


def _shift(x, axis, n, step):
    return lax.ppermute(x, axis, perm=[(i, (i + step) % n) for i in range(n)])


def ring_gather(x, axis, n):
    ahead = n // 2
    behind = n - 1 - ahead
    out = [None] * n
    out[0] = x
    fwd = x
    bwd = x
    for s in range(1, ahead + 1):
        fwd = _shift(fwd, axis, n, 1)
        out[(n - s) % n] = fwd
        if s <= behind:
            bwd = _shift(bwd, axis, n, -1)
            out[s] = bwd
    return out


def ring_sum_scatter(parts, axis, n):
    ahead = n // 2
    behind = n - 1 - ahead
    fwd = parts[ahead]
    bwd = parts[(n - behind) % n] if behind > 0 else None
    for s in range(1, ahead + 1):
        fwd = _shift(fwd, axis, n, 1)
        total = fwd.astype(F32) + parts[ahead - s].astype(F32)
        fwd = total.astype(BF16) if s < ahead else total
        if s <= behind:
            bwd = _shift(bwd, axis, n, -1)
            if s < behind:
                bwd = (bwd.astype(F32) + parts[(s - behind) % n].astype(F32)).astype(BF16)
    if bwd is None:
        return fwd
    return fwd + bwd.astype(F32)


def _halves(x, half):
    return x[..., :half], x[..., half:]


def ring4_gather(x, axis, half):
    n = 4
    from_left = _shift(x, axis, n, 1)
    from_right = _shift(x, axis, n, -1)
    far_a = _shift(_halves(from_left, half)[0], axis, n, 1)
    far_b = _shift(_halves(from_right, half)[1], axis, n, -1)
    return [x, from_right, jnp.concatenate([far_a, far_b], axis=-1), from_left]


def ring4_sum_scatter(parts, axis, half):
    n = 4
    own_a, own_b = _halves(parts[0], half)
    next_a, next_b = _halves(parts[1], half)
    far_a, far_b = _halves(parts[2], half)
    prev_a, prev_b = _halves(parts[3], half)
    got_left = _shift(jnp.concatenate([far_a, next_b], axis=-1), axis, n, 1)
    got_right = _shift(jnp.concatenate([prev_a, far_b], axis=-1), axis, n, -1)
    left_a, left_b = _halves(got_left, half)
    right_a, right_b = _halves(got_right, half)
    send_a = (left_a.astype(F32) + next_a.astype(F32)).astype(BF16)
    send_b = (right_b.astype(F32) + prev_b.astype(F32)).astype(BF16)
    two_left = _shift(send_a, axis, n, 1)
    two_right = _shift(send_b, axis, n, -1)
    total_a = own_a.astype(F32) + two_left.astype(F32) + right_a.astype(F32)
    total_b = own_b.astype(F32) + two_right.astype(F32) + left_b.astype(F32)
    return jnp.concatenate([total_a, total_b], axis=-1)


def on_device(layer_input, hidden_grad, gate_slots, up_slots, block_mask):
    n_dp = lax.axis_size("dp")
    n_row = lax.axis_size("row")
    n_col = lax.axis_size("col")
    k_dp = lax.axis_index("dp")
    k_row = lax.axis_index("row")
    k_col = lax.axis_index("col")
    bs = gate_slots.shape[-1]
    per_dev = gate_slots.shape[2]
    cap = per_dev * n_dp
    feat = layer_input.shape[1]
    units = hidden_grad.shape[1]
    tile_rows = feat // bs
    tile_cols = units // bs
    tok = layer_input.shape[0] * n_col
    rows_per = tok // n_row
    cols_per = tok // n_col

    pair_local = jnp.concatenate([gate_slots[0, 0], up_slots[0, 0]], axis=2)
    pair_local = pair_local.reshape(per_dev * bs, 2 * bs)
    pair_all = lax.all_gather(pair_local, "dp", axis=0, tiled=True).reshape(cap, bs, 2 * bs)

    x_rel = jnp.stack(ring_gather(layer_input, "col", n_col))
    x_abs = jnp.roll(x_rel, k_col, axis=0).reshape(tok, tile_rows, bs)

    tile_mask = lax.dynamic_slice(
        block_mask, (k_row * tile_rows, k_col * tile_cols), (tile_rows, tile_cols)
    ).reshape(tile_rows * tile_cols)
    kept = tile_mask > 0
    position = jnp.cumsum(kept.astype(jnp.int32)) - 1
    q = jnp.arange(cap, dtype=jnp.int32)
    picks = kept[None, :] & (position[None, :] == q[:, None])
    onehot3 = picks.astype(BF16).reshape(cap, tile_rows, tile_cols)
    row_pick = jnp.sum(onehot3, axis=2)
    col_pick = jnp.sum(onehot3, axis=1)
    highest = lax.Precision.HIGH

    x_pick = jnp.einsum("qr,trk->qtk", row_pick, x_abs, preferred_element_type=F32).astype(BF16)
    by_col = jnp.einsum(
        "qcr,qkn->ckrn", onehot3.transpose(0, 2, 1), pair_all, preferred_element_type=F32
    ).astype(BF16).reshape(tile_cols, feat, 2 * bs)
    x_kr = x_abs.transpose(0, 2, 1).reshape(1, tok, feat)
    x_wide = jnp.broadcast_to(x_kr, (tile_cols, tok, feat))
    pre = lax.dot_general(
        x_wide, by_col, (((2,), (1,)), ((0,), (0,))), preferred_element_type=F32
    ).astype(BF16)
    pre_roll = jnp.roll(pre.reshape(tile_cols, n_row, rows_per, 2 * bs), -k_row, axis=1)
    if n_row == 4:
        pre_sum = ring4_sum_scatter([pre_roll[:, m] for m in range(n_row)], "row", bs)
    else:
        pre_sum = ring_sum_scatter([pre_roll[:, m] for m in range(n_row)], "row", n_row)
    gate = pre_sum[..., :bs]
    up = pre_sum[..., bs:]
    upstream = hidden_grad.astype(F32).reshape(rows_per, tile_cols, bs).transpose(1, 0, 2)
    sig = jax.nn.sigmoid(gate)
    gate_grad = (upstream * up * sig * (1.0 + gate * (1.0 - sig))).astype(BF16)
    up_grad = (upstream * gate * sig).astype(BF16)
    grad_local = jnp.concatenate([gate_grad, up_grad], axis=2)
    if n_row == 4:
        grad_rel = jnp.stack(ring4_gather(grad_local, "row", bs), axis=1)
    else:
        grad_rel = jnp.stack(ring_gather(grad_local, "row", n_row), axis=1)
    grad_rel = grad_rel.reshape(tile_cols, tok, 2 * bs)
    x_pick_rel = jnp.roll(x_pick.reshape(cap, n_row, rows_per, bs), -k_row, axis=1)
    x_pick_rel = x_pick_rel.reshape(cap, tok, bs)

    g_pick = jnp.einsum("qc,ctn->qtn", col_pick, grad_rel, preferred_element_type=F32).astype(BF16)
    slot_dw = jnp.einsum("qtk,qtn->qkn", x_pick_rel, g_pick, preferred_element_type=F32).astype(BF16)

    dx_slot = jnp.einsum("qtn,qkn->qtk", g_pick, pair_all, preferred_element_type=F32)
    dx = jnp.einsum(
        "qr,qtk->rtk", row_pick.astype(F32), dx_slot, precision=highest, preferred_element_type=F32
    ).astype(BF16)
    dx = jnp.roll(dx.reshape(tile_rows, n_row, rows_per, bs), k_row, axis=1)
    dx_roll = jnp.roll(dx.reshape(tile_rows, n_col, cols_per, bs), -k_col, axis=1)
    dx_sum = ring_sum_scatter([dx_roll[:, m] for m in range(n_col)], "col", n_col)
    input_grad = dx_sum.transpose(1, 0, 2).reshape(cols_per, feat).astype(BF16)

    dw_sum = lax.psum_scatter(
        slot_dw.reshape(cap * bs, 2 * bs), "dp", scatter_dimension=0, tiled=True
    ).astype(F32) / n_dp
    dw_sum = dw_sum.reshape(per_dev, bs, 2 * bs)
    gate_out = dw_sum[..., :bs][None, None]
    up_out = dw_sum[..., bs:][None, None]
    return (input_grad, gate_out, up_out)


def solution(mesh):
    return jax.shard_map(
        on_device,
        mesh=mesh,
        in_specs=(
            P(("dp", "col"), "row"),
            P(("dp", "row"), "col"),
            P("row", "col", "dp", None, None),
            P("row", "col", "dp", None, None),
            P(),
        ),
        out_specs=(
            P(("dp", "col"), "row"),
            P("row", "col", "dp", None, None),
            P("row", "col", "dp", None, None),
        ),
        check_vma=False,
    )
```
